32 devices in a mesh: ctx: 16 (over z, y, x), head: 2 (over core).
Axes of the slice: x: 2, y: 2, z: 4, core: 2. Of those that a mesh axis runs over, the one named last changes fastest.
Arguments:
- activations: bfloat16 [7168, 4096], P('ctx'), may hold values from -150 to 150
- query_weight: bfloat16 [4096, 2048], P('ctx', 'head'), may hold values from -0.09375 to 0.09375
- keyval_weight: bfloat16 [4096, 2, 2048], P('ctx', None, 'head'), may hold values from -0.09375 to 0.09375
- out_weight: bfloat16 [2048, 4096], P('head', 'ctx'), may hold values from -0.125 to 0.125
- norm_gain: float32 [4096], replicated, may hold values from 0.1 to 1.9
- vocab_weight: bfloat16 [63488, 4096], P(('ctx', 'head')), may hold values from -15 to 15
- mask_positions: int32 [16, 16], P('ctx'), may hold values from 0 to 447, as said below
- mask_count: int32 [16], P('ctx'), may hold values from 1 to 16, as said below
- targets: int32 [16, 16], P('ctx'), may hold values from 0 to 63487
Outputs:
- loss: float32 [16, 16], P('ctx')
The draws below stay inside these ranges and needn't reach their ends.
Inputs may be any that keep to these rules, and one draw needn't show every extreme that they name: `mask_positions`: the 16 entries of a row are distinct; the first mask_count[c] of row c are the masked positions of block c, the others unused. `mask_count`: some block has all 16 slots used.
All inputs are finite; a program needn't handle non-finite values.
Results may differ from the reference program's by a relative error of at most 0.0098.
Values may be sent and summed in bfloat16 or wider, within the bound.
No kernel may reach another device: no remote copies, remote signals or barrier semaphores. Data moves between devices by JAX's collectives and lax.ppermute only.
A program may use at most 128 MiB of HBM per device.

```python
import math
import jax
import jax.numpy as jnp
import numpy as np
from jax import lax

D = 4096
HEADS = 16
HDIM = 128
V = 63488
CB = 448
MSK = 16
SEQ = 7168
ROWS = 256
N_CTX = 16


def draw_activations(key, part):
    key_base = jax.random.fold_in(key, 0)
    normal_part = jnp.clip(jax.random.normal(key_base, (CB * N_CTX, D), jnp.float32), -5.0, 5.0)
    row_ramp = 0.6 + 1.2 * jnp.arange(CB * N_CTX, dtype=jnp.float32) / (CB * N_CTX)
    return (normal_part * row_ramp[:, None]).astype(jnp.bfloat16)


def draw_vocab_weight(key, part):
    key_base = jax.random.fold_in(key, 0)
    normal_part = jnp.clip(jax.random.normal(key_base, (V, D), jnp.float32), -5.0, 5.0)
    row_ramp = (0.5 + jnp.arange(V, dtype=jnp.float32) / V) * (3.0 / math.sqrt(D))
    return jnp.clip(normal_part * row_ramp[:, None], -15.0, 15.0).astype(jnp.bfloat16)


def place_value(layout_table, row_index, slot_index, new_value):
    row_values = layout_table[row_index]
    present = row_values[slot_index]
    repaired = jnp.where(row_values == new_value, present, row_values)
    repaired = repaired.at[slot_index].set(new_value)
    return layout_table.at[row_index].set(repaired)


def masked_layout(key):
    base_key = jax.random.fold_in(key, 7)
    key_count, key_full, key_perm, key_low = jax.random.split(base_key, 4)
    counts = jax.random.randint(key_count, (N_CTX,), 1, MSK + 1)
    full_block = jax.random.randint(key_full, (), 0, N_CTX)
    counts = jnp.where(jnp.arange(N_CTX) == full_block, MSK, counts).astype(jnp.int32)
    row_keys = jax.random.split(key_perm, N_CTX)
    layout_table = jax.vmap(lambda row_key: jax.random.permutation(row_key, CB))(row_keys).astype(jnp.int32)
    low_block = jax.random.randint(key_low, (), 0, N_CTX)
    layout_table = place_value(layout_table, full_block, 0, CB - 1)
    layout_table = place_value(layout_table, low_block, 0, 0)
    layout_table = place_value(layout_table, full_block, 0, CB - 1)
    return (layout_table[:, :MSK], counts)


def draw_mask_positions(key, part):
    return masked_layout(key)[0]


def draw_mask_count(key, part):
    return masked_layout(key)[1]


def plant(drawn, key, smallest, top_value):
    place = [jax.random.randint(jax.random.fold_in(key, axis), (), 0, length) for axis, length in enumerate(drawn.shape)]
    longest = drawn.shape.index(max(drawn.shape))
    neighbour = place[:longest] + [(place[longest] + 1) % drawn.shape[longest]] + place[longest + 1:]
    return drawn.at[tuple(place)].set(smallest).at[tuple(neighbour)].set(top_value)


def steps_of(rng, shape, shards, least, top_value):
    loudness, own = 1.0, jax.random.fold_in(rng, 6)
    for axis_at, shards_of in shards:
        draws = jnp.exp(jax.random.uniform(jax.random.fold_in(own, axis_at), (shards_of,), jnp.float32, least / len(shards), top_value / len(shards)))
        loudness = loudness * jnp.repeat(draws, shape[axis_at] // shards_of).reshape([-1 if axis == axis_at else 1 for axis in range(len(shape))])
    return loudness


def rank_table(count, slope):
    weights = [(1 << 20) // math.isqrt(grade ** slope) + 1 for grade in range(1, count + 1)]
    scale = 1 + sum(weights) // (1 << 30)
    return np.cumsum(np.array([max(1, weight // scale) for weight in weights]))


def ranked(stream_key, dims, number_of, slope):
    listing = rank_table(number_of, slope)
    ticket = jax.random.randint(jax.random.fold_in(stream_key, 1), dims, 0, int(listing[number_of - 1]))
    standing = jnp.searchsorted(jnp.asarray(listing, jnp.int32), ticket, side="right")
    return jax.random.permutation(jax.random.fold_in(stream_key, 2), number_of)[standing].astype(jnp.int32)


def bell_draw(stream_key, dims, width, reach, cuts=(), kind=jnp.bfloat16):
    array = jax.random.normal(stream_key, dims, jnp.float32) * width
    if len(cuts) > 0:
        array = steps_of(stream_key, dims, cuts, -0.22, 0.18) * array
    return jnp.clip(array, min=-reach, max=reach).astype(kind)


def setup_inputs(seed: int = 0) -> dict:
    seeds = jax.random.split(jax.random.key(seed), 10)
    activations = draw_activations(jax.random.fold_in(seeds[9], 71), 0)
    query_weight = bell_draw(seeds[1], (D, HEADS * HDIM), D ** -0.5, 0.09375, ((0, 16), (1, 2)))
    keyval_weight = bell_draw(seeds[2], (D, 2, HEADS * HDIM), D ** -0.5, 0.09375, ((0, 16), (2, 2)))
    out_weight = bell_draw(seeds[3], (HEADS * HDIM, D), (HEADS * HDIM) ** -0.5, 0.125, ((0, 2), (1, 16)))
    norm_gain = jnp.clip(1.0 + 0.18 * jax.random.normal(seeds[4], (D,), jnp.float32), 0.1, 1.9)
    vocab_weight = draw_vocab_weight(jax.random.fold_in(seeds[9], 71), 0)
    mask_positions = draw_mask_positions(jax.random.fold_in(seeds[9], 71), 0)
    mask_count = draw_mask_count(jax.random.fold_in(seeds[9], 71), 0)
    targets = plant(ranked(seeds[8], (N_CTX, MSK), V, 2), jax.random.fold_in(seeds[8], 3), 0, V - 1).astype(jnp.int32)
    return dict(activations=activations, query_weight=query_weight, keyval_weight=keyval_weight, out_weight=out_weight, norm_gain=norm_gain, vocab_weight=vocab_weight, mask_positions=mask_positions, mask_count=mask_count, targets=targets)


def one_head(triple):
    query_rows, key_rows, value_rows = triple
    scores = jnp.dot(query_rows, key_rows.T, preferred_element_type=jnp.float32) * HDIM ** (-0.5)
    highest = lax.optimization_barrier(jnp.max(scores, axis=1, keepdims=True))
    exponent = jnp.exp(scores - highest)
    numerator = jnp.dot(exponent.astype(jnp.bfloat16), value_rows, preferred_element_type=jnp.float32)
    return numerator / lax.optimization_barrier(jnp.sum(exponent, axis=1, keepdims=True))

def reference(activations, query_weight, keyval_weight, out_weight, norm_gain, vocab_weight, mask_positions, mask_count, targets):
    attn_width = HEADS * HDIM
    keyval = jnp.dot(activations, keyval_weight.reshape(D, 2 * attn_width), preferred_element_type=jnp.float32).astype(jnp.bfloat16)
    key_heads = keyval[:, :attn_width].reshape(SEQ, HEADS, HDIM).transpose(1, 0, 2)
    value_heads = keyval[:, attn_width:].reshape(SEQ, HEADS, HDIM).transpose(1, 0, 2)
    offsets = jnp.arange(N_CTX, dtype=jnp.int32)[:, None] * CB
    positions = (offsets + mask_positions).reshape(ROWS)
    picked_rows = jnp.take(activations, positions, axis=0)
    queries = jnp.dot(picked_rows, query_weight, preferred_element_type=jnp.float32).astype(jnp.bfloat16)
    queries = queries.reshape(ROWS, HEADS, HDIM).transpose(1, 0, 2)
    per_head = lax.map(one_head, (queries, key_heads, value_heads))
    attended = per_head.transpose(1, 0, 2).reshape(ROWS, attn_width).astype(jnp.bfloat16)
    branch = jnp.dot(attended, out_weight, preferred_element_type=jnp.float32)
    meansquare = lax.optimization_barrier(jnp.mean(branch * branch, axis=1, keepdims=True))
    hidden = (branch * lax.rsqrt(meansquare + 1e-06) * norm_gain).astype(jnp.bfloat16)
    logits = jnp.dot(hidden, vocab_weight.T, preferred_element_type=jnp.float32)
    highest = lax.optimization_barrier(jnp.max(logits, axis=1))
    expsum = lax.optimization_barrier(jnp.sum(jnp.exp(logits - highest[:, None]), axis=1))
    wanted = targets.reshape(ROWS)
    picked = jnp.take_along_axis(logits, wanted[:, None], axis=1)[:, 0]
    losses = (highest + jnp.log(expsum) - picked).reshape(N_CTX, MSK)
    active = jnp.arange(MSK, dtype=jnp.int32)[None, :] < mask_count[:, None]
    return jnp.where(active, losses, jnp.zeros_like(losses))
```

```python
import jax
import jax.numpy as jnp
from jax import lax
from jax.sharding import PartitionSpec as P

HDIM = 128


def _bits(n):
    b = n.bit_length() - 1
    assert 1 << b == n
    return b


def _swap(x, axis, n, k):
    return lax.ppermute(x, axis, [(j, j ^ k) for j in range(n)])


def _all_reduce(x, axis, n, combine):
    k = 1
    while k < n:
        x = combine(x, _swap(x, axis, n, k))
        k *= 2
    return x


def _reduce_scatter(x, axis, n, combine):
    nb = _bits(n)
    idx = lax.axis_index(axis)
    rest = x.shape[1:]
    x = x.reshape((2,) * nb + rest)
    for p in range(nb):
        pos = nb - 1 - p
        bit = (idx // (1 << p)) % 2
        keep = lax.dynamic_index_in_dim(x, bit, pos, keepdims=False)
        send = lax.dynamic_index_in_dim(x, 1 - bit, pos, keepdims=False)
        x = combine(keep, _swap(send, axis, n, 1 << p))
    return x


def _all_gather(x, axis, n):
    nb = _bits(n)
    idx = lax.axis_index(axis)
    rest = x.shape
    for r, p in enumerate(reversed(range(nb))):
        y = _swap(x, axis, n, 1 << p)
        bit = (idx // (1 << p)) % 2
        x = jnp.where(bit == 0, jnp.stack([x, y], axis=r), jnp.stack([y, x], axis=r))
    return x.reshape((n,) + rest)


def _add(a, b):
    return a + b


def shards(
    activations,
    query_weight,
    keyval_weight,
    out_weight,
    norm_gain,
    vocab_weight,
    mask_positions,
    mask_count,
    targets,
):
    n_ctx = lax.axis_size("ctx")
    n_head = lax.axis_size("head")
    block_len = activations.shape[0]
    width = activations.shape[1]
    slot_count = mask_positions.shape[1]
    total_rows = n_ctx * slot_count
    head_columns = query_weight.shape[1]
    heads_here = head_columns // HDIM
    in_rows = query_weight.shape[0]
    col_block = out_weight.shape[1]

    kv_weight = lax.all_gather(keyval_weight, "ctx", axis=0, tiled=True)

    rows_here = jnp.take(activations, mask_positions[0], axis=0)
    row_blocks = lax.all_to_all(rows_here, "ctx", 1, 0, tiled=True)
    partial_q = jnp.dot(row_blocks, query_weight, preferred_element_type=jnp.float32)
    own_q = _reduce_scatter(
        partial_q.reshape(n_ctx, slot_count, head_columns), "ctx", n_ctx, _add
    ).astype(jnp.bfloat16)
    queries = _all_gather(own_q, "ctx", n_ctx).reshape(total_rows, head_columns)

    wanted = _all_gather(targets[0], "ctx", n_ctx).reshape(total_rows)
    out_full = _all_gather(out_weight, "head", n_head).reshape(n_head * head_columns, col_block)

    keyval = jnp.einsum(
        "td,djc->tjc", activations, kv_weight, preferred_element_type=jnp.float32
    ).astype(jnp.bfloat16)
    key_heads = keyval[:, 0].reshape(block_len, heads_here, HDIM)
    value_heads = keyval[:, 1].reshape(block_len, heads_here, HDIM)
    query_heads = queries.reshape(total_rows, heads_here, HDIM)
    scores = jnp.einsum(
        "rhc,thc->hrt", query_heads, key_heads, preferred_element_type=jnp.float32
    ) * HDIM ** (-0.5)
    local_top = jnp.max(scores, axis=2)
    exponent = jnp.exp(scores - local_top[:, :, None])
    weights = exponent.astype(jnp.bfloat16)
    numerator = jnp.einsum(
        "hrt,thc->rhc", weights, value_heads, preferred_element_type=jnp.float32
    ).reshape(total_rows, head_columns)
    denominator = jnp.sum(exponent, axis=2).T
    packed = jnp.concatenate([numerator, local_top.T, denominator], axis=1)

    def att_combine(a, b):
        na, ma, da = jnp.split(a, [head_columns, head_columns + heads_here], axis=-1)
        nb_, mb, db = jnp.split(b, [head_columns, head_columns + heads_here], axis=-1)
        top = jnp.maximum(ma, mb)
        sa = jnp.exp(ma - top)
        sb = jnp.exp(mb - top)
        lead = na.shape[:-1]
        num = (
            na.reshape(lead + (heads_here, HDIM)) * sa[..., None]
            + nb_.reshape(lead + (heads_here, HDIM)) * sb[..., None]
        ).reshape(lead + (head_columns,))
        return jnp.concatenate([num, top, da * sa + db * sb], axis=-1)

    combined = _reduce_scatter(
        packed.reshape(n_ctx, slot_count, packed.shape[1]), "ctx", n_ctx, att_combine
    )
    num = combined[:, :head_columns].reshape(slot_count, heads_here, HDIM)
    den = combined[:, head_columns + heads_here :]
    attended = (num / den[:, :, None]).reshape(slot_count, head_columns).astype(jnp.bfloat16)
    attended = _all_gather(attended, "ctx", n_ctx).reshape(total_rows, head_columns)
    attended = _all_gather(attended, "head", n_head)
    attended = attended.transpose(1, 0, 2).reshape(total_rows, n_head * head_columns)

    share = total_rows // n_head
    head_idx = lax.axis_index("head")
    my_rows = lax.dynamic_slice_in_dim(attended, head_idx * share, share, 0)
    branch = jnp.dot(my_rows, out_full, preferred_element_type=jnp.float32)
    sumsq = _all_reduce(jnp.sum(branch * branch, axis=1), "ctx", n_ctx, _add)
    gain = lax.dynamic_slice_in_dim(norm_gain, lax.axis_index("ctx") * col_block, col_block, 0)
    hidden = (
        branch * lax.rsqrt(sumsq / width + 1e-06)[:, None] * gain
    ).astype(jnp.bfloat16)
    hidden = _all_gather(hidden, "ctx", n_ctx).transpose(1, 0, 2).reshape(share, width)
    hidden = _all_gather(hidden, "head", n_head).reshape(total_rows, width)

    logits = lax.dot_general(
        hidden, vocab_weight, (((1,), (1,)), ((), ())), preferred_element_type=jnp.float32
    )
    vocab_start = lax.axis_index(("ctx", "head")) * vocab_weight.shape[0]
    vocab_ids = vocab_start + jnp.arange(vocab_weight.shape[0], dtype=jnp.int32)
    local_max = jnp.max(logits, axis=1)
    expsum = jnp.sum(jnp.exp(logits - local_max[:, None]), axis=1)
    picked = jnp.sum(jnp.where(vocab_ids[None, :] == wanted[:, None], logits, 0.0), axis=1)
    stats = jnp.stack([local_max, expsum, picked])

    def lse_combine(a, b):
        top = jnp.maximum(a[0], b[0])
        total = a[1] * jnp.exp(a[0] - top) + b[1] * jnp.exp(b[0] - top)
        return jnp.stack([top, total, a[2] + b[2]])

    stats = _all_reduce(stats, "head", n_head, lse_combine)
    stats = _all_reduce(stats, "ctx", n_ctx, lse_combine)
    losses = (stats[0] + jnp.log(stats[1]) - stats[2]).reshape(n_ctx, slot_count)
    block_losses = lax.dynamic_slice_in_dim(losses, lax.axis_index("ctx"), 1, 0)[0]
    active = jnp.arange(slot_count, dtype=jnp.int32) < mask_count[0]
    return jnp.where(active, block_losses, jnp.zeros_like(block_losses))[None, :]


def solution(mesh):
    in_specs = (
        P("ctx", None),
        P("ctx", "head"),
        P("ctx", None, "head"),
        P("head", "ctx"),
        P(),
        P(("ctx", "head"), None),
        P("ctx", None),
        P("ctx"),
        P("ctx", None),
    )
    out_specs = P("ctx", None)
    return jax.shard_map(shards, mesh=mesh, in_specs=in_specs, out_specs=out_specs, check_vma=False)
```

```python
import jax
import jax.numpy as jnp
from jax import lax
from jax.sharding import PartitionSpec as P

HDIM = 128


def _digits(n):
    b = n.bit_length() - 1
    assert 1 << b == n
    out, p = [], 0
    while p < b:
        r = 4 if b - p >= 2 else 2
        out.append((p, r))
        p += r.bit_length() - 1
    return out


def _swap(x, axis, n, k):
    return lax.ppermute(x, axis, [(j, j ^ k) for j in range(n)])


def _exchange(x_for, axis, n, p, r, digit):
    return [None] + [_swap(x_for(s), axis, n, s << p) for s in range(1, r)]


def _all_reduce(x, axis, n, combine):
    idx = lax.axis_index(axis)
    for p, r in _digits(n):
        digit = (idx // (1 << p)) % r
        got = _exchange(lambda s: x, axis, n, p, r, digit)
        got[0] = x
        stacked = jnp.stack(got)
        acc = lax.dynamic_index_in_dim(stacked, digit, 0, keepdims=False)
        for a in range(1, r):
            acc = combine(acc, lax.dynamic_index_in_dim(stacked, a ^ digit, 0, keepdims=False))
        x = acc
    return x


def _reduce_scatter(x, axis, n, combine):
    idx = lax.axis_index(axis)
    rest = x.shape[1:]
    for p, r in _digits(n):
        digit = (idx // (1 << p)) % r
        x = x.reshape((x.shape[0] // r, r) + rest)
        got = _exchange(
            lambda s: lax.dynamic_index_in_dim(x, digit ^ s, 1, keepdims=False),
            axis, n, p, r, digit,
        )
        acc = lax.dynamic_index_in_dim(x, digit, 1, keepdims=False)
        for s in range(1, r):
            acc = combine(acc, got[s])
        x = acc
    return x[0]


def _all_gather(x, axis, n):
    idx = lax.axis_index(axis)
    rest = x.shape
    for k, (p, r) in enumerate(reversed(_digits(n))):
        digit = (idx // (1 << p)) % r
        got = _exchange(lambda s: x, axis, n, p, r, digit)
        got[0] = x
        stacked = jnp.stack(got)
        x = jnp.stack(
            [lax.dynamic_index_in_dim(stacked, a ^ digit, 0, keepdims=False) for a in range(r)],
            axis=k,
        )
    return x.reshape((n,) + rest)


def _add(a, b):
    return a + b


def shards(
    activations,
    query_weight,
    keyval_weight,
    out_weight,
    norm_gain,
    vocab_weight,
    mask_positions,
    mask_count,
    targets,
):
    n_ctx = lax.axis_size("ctx")
    n_head = lax.axis_size("head")
    block_len = activations.shape[0]
    width = activations.shape[1]
    slot_count = mask_positions.shape[1]
    total_rows = n_ctx * slot_count
    head_columns = query_weight.shape[1]
    heads_here = head_columns // HDIM
    in_rows = query_weight.shape[0]
    col_block = out_weight.shape[1]

    kv_weight = lax.all_gather(keyval_weight, "ctx", axis=0, tiled=True)

    rows_here = jnp.take(activations, mask_positions[0], axis=0)
    row_blocks = lax.all_to_all(rows_here, "ctx", 1, 0, tiled=True)
    partial_q = jnp.dot(row_blocks, query_weight, preferred_element_type=jnp.float32)
    own_q = _reduce_scatter(
        partial_q.reshape(n_ctx, slot_count, head_columns), "ctx", n_ctx, _add
    ).astype(jnp.bfloat16)
    queries = _all_gather(own_q, "ctx", n_ctx).reshape(total_rows, head_columns)

    wanted = _all_gather(targets[0], "ctx", n_ctx).reshape(total_rows)
    out_full = _all_gather(out_weight, "head", n_head).reshape(n_head * head_columns, col_block)

    keyval = jnp.einsum(
        "td,djc->tjc", activations, kv_weight, preferred_element_type=jnp.float32
    ).astype(jnp.bfloat16)
    key_heads = keyval[:, 0].reshape(block_len, heads_here, HDIM)
    value_heads = keyval[:, 1].reshape(block_len, heads_here, HDIM)
    query_heads = queries.reshape(total_rows, heads_here, HDIM)
    scores = jnp.einsum(
        "rhc,thc->hrt", query_heads, key_heads, preferred_element_type=jnp.float32
    ) * HDIM ** (-0.5)
    local_top = jnp.max(scores, axis=2)
    exponent = jnp.exp(scores - local_top[:, :, None])
    weights = exponent.astype(jnp.bfloat16)
    numerator = jnp.einsum(
        "hrt,thc->rhc", weights, value_heads, preferred_element_type=jnp.float32
    ).reshape(total_rows, head_columns)
    denominator = jnp.sum(exponent, axis=2).T
    packed = jnp.concatenate([numerator, local_top.T, denominator], axis=1)

    def att_combine(a, b):
        na, ma, da = jnp.split(a, [head_columns, head_columns + heads_here], axis=-1)
        nb_, mb, db = jnp.split(b, [head_columns, head_columns + heads_here], axis=-1)
        top = jnp.maximum(ma, mb)
        sa = jnp.exp(ma - top)
        sb = jnp.exp(mb - top)
        lead = na.shape[:-1]
        num = (
            na.reshape(lead + (heads_here, HDIM)) * sa[..., None]
            + nb_.reshape(lead + (heads_here, HDIM)) * sb[..., None]
        ).reshape(lead + (head_columns,))
        return jnp.concatenate([num, top, da * sa + db * sb], axis=-1)

    combined = _reduce_scatter(
        packed.reshape(n_ctx, slot_count, packed.shape[1]), "ctx", n_ctx, att_combine
    )
    num = combined[:, :head_columns].reshape(slot_count, heads_here, HDIM)
    den = combined[:, head_columns + heads_here :]
    attended = (num / den[:, :, None]).reshape(slot_count, head_columns).astype(jnp.bfloat16)
    attended = _all_gather(attended, "ctx", n_ctx).reshape(total_rows, head_columns)
    attended = _all_gather(attended, "head", n_head)
    attended = attended.transpose(1, 0, 2).reshape(total_rows, n_head * head_columns)

    share = total_rows // n_head
    head_idx = lax.axis_index("head")
    my_rows = lax.dynamic_slice_in_dim(attended, head_idx * share, share, 0)
    branch = jnp.dot(my_rows, out_full, preferred_element_type=jnp.float32)
    sumsq = _all_reduce(jnp.sum(branch * branch, axis=1), "ctx", n_ctx, _add)
    gain = lax.dynamic_slice_in_dim(norm_gain, lax.axis_index("ctx") * col_block, col_block, 0)
    hidden = (
        branch * lax.rsqrt(sumsq / width + 1e-06)[:, None] * gain
    ).astype(jnp.bfloat16)
    hidden = _all_gather(hidden, "ctx", n_ctx).transpose(1, 0, 2).reshape(share, width)
    hidden = _all_gather(hidden, "head", n_head).reshape(total_rows, width)

    logits = lax.dot_general(
        hidden, vocab_weight, (((1,), (1,)), ((), ())), preferred_element_type=jnp.float32
    )
    vocab_start = lax.axis_index(("ctx", "head")) * vocab_weight.shape[0]
    vocab_ids = vocab_start + jnp.arange(vocab_weight.shape[0], dtype=jnp.int32)
    local_max = jnp.max(logits, axis=1)
    expsum = jnp.sum(jnp.exp(logits - local_max[:, None]), axis=1)
    picked = jnp.sum(jnp.where(vocab_ids[None, :] == wanted[:, None], logits, 0.0), axis=1)
    stats = jnp.stack([local_max, expsum, picked])

    def lse_combine(a, b):
        top = jnp.maximum(a[0], b[0])
        total = a[1] * jnp.exp(a[0] - top) + b[1] * jnp.exp(b[0] - top)
        return jnp.stack([top, total, a[2] + b[2]])

    stats = _all_reduce(stats, "head", n_head, lse_combine)
    stats = _all_reduce(stats, "ctx", n_ctx, lse_combine)
    losses = (stats[0] + jnp.log(stats[1]) - stats[2]).reshape(n_ctx, slot_count)
    block_losses = lax.dynamic_slice_in_dim(losses, lax.axis_index("ctx"), 1, 0)[0]
    active = jnp.arange(slot_count, dtype=jnp.int32) < mask_count[0]
    return jnp.where(active, block_losses, jnp.zeros_like(block_losses))[None, :]


def solution(mesh):
    in_specs = (
        P("ctx", None),
        P("ctx", "head"),
        P("ctx", None, "head"),
        P("head", "ctx"),
        P(),
        P(("ctx", "head"), None),
        P("ctx", None),
        P("ctx"),
        P("ctx", None),
    )
    out_specs = P("ctx", None)
    return jax.shard_map(shards, mesh=mesh, in_specs=in_specs, out_specs=out_specs, check_vma=False)
```

```python
import jax
import jax.numpy as jnp
from jax import lax
from jax.sharding import PartitionSpec as P

HDIM = 128


def _digits(n):
    b = n.bit_length() - 1
    assert 1 << b == n
    out, p = [], 0
    while p < b:
        r = 4 if b - p >= 2 else 2
        out.append((p, r))
        p += r.bit_length() - 1
    return out


def _swap(x, axis, n, k):
    return lax.ppermute(x, axis, [(j, j ^ k) for j in range(n)])


def _exchange(x_for, axis, n, p, r, digit):
    return [None] + [_swap(x_for(s), axis, n, s << p) for s in range(1, r)]


def _all_reduce(x, axis, n, combine):
    idx = lax.axis_index(axis)
    for p, r in _digits(n):
        digit = (idx // (1 << p)) % r
        got = _exchange(lambda s: x, axis, n, p, r, digit)
        got[0] = x
        stacked = jnp.stack(got)
        acc = lax.dynamic_index_in_dim(stacked, digit, 0, keepdims=False)
        for a in range(1, r):
            acc = combine(acc, lax.dynamic_index_in_dim(stacked, a ^ digit, 0, keepdims=False))
        x = acc
    return x


def _reduce_scatter(x, axis, n, combine):
    idx = lax.axis_index(axis)
    rest = x.shape[1:]
    for p, r in _digits(n):
        digit = (idx // (1 << p)) % r
        x = x.reshape((x.shape[0] // r, r) + rest)
        got = _exchange(
            lambda s: lax.dynamic_index_in_dim(x, digit ^ s, 1, keepdims=False),
            axis, n, p, r, digit,
        )
        acc = lax.dynamic_index_in_dim(x, digit, 1, keepdims=False)
        for s in range(1, r):
            acc = combine(acc, got[s])
        x = acc
    return x[0]


def _all_gather(x, axis, n):
    idx = lax.axis_index(axis)
    rest = x.shape
    for k, (p, r) in enumerate(reversed(_digits(n))):
        digit = (idx // (1 << p)) % r
        got = _exchange(lambda s: x, axis, n, p, r, digit)
        got[0] = x
        stacked = jnp.stack(got)
        x = jnp.stack(
            [lax.dynamic_index_in_dim(stacked, a ^ digit, 0, keepdims=False) for a in range(r)],
            axis=k,
        )
    return x.reshape((n,) + rest)


def _add(a, b):
    return a + b


def shards(
    activations,
    query_weight,
    keyval_weight,
    out_weight,
    norm_gain,
    vocab_weight,
    mask_positions,
    mask_count,
    targets,
):
    n_ctx = lax.axis_size("ctx")
    n_head = lax.axis_size("head")
    block_len = activations.shape[0]
    width = activations.shape[1]
    slot_count = mask_positions.shape[1]
    total_rows = n_ctx * slot_count
    head_columns = query_weight.shape[1]
    heads_here = head_columns // HDIM
    in_rows = query_weight.shape[0]
    col_block = out_weight.shape[1]

    kv_weight = lax.all_gather(keyval_weight, "ctx", axis=0, tiled=True)

    rows_here = jnp.take(activations, mask_positions[0], axis=0)
    row_blocks = lax.all_to_all(rows_here, "ctx", 1, 0, tiled=True)
    partial_q = jnp.dot(row_blocks, query_weight, preferred_element_type=jnp.float32)
    own_q = _reduce_scatter(
        partial_q.reshape(n_ctx, slot_count, head_columns), "ctx", n_ctx, _add
    ).astype(jnp.bfloat16)
    queries = _all_gather(own_q, "ctx", n_ctx).reshape(total_rows, head_columns)

    wanted = _all_gather(targets[0], "ctx", n_ctx).reshape(total_rows)
    out_full = _all_gather(out_weight, "head", n_head).reshape(n_head * head_columns, col_block)

    keyval = jnp.einsum(
        "td,djc->tjc", activations, kv_weight, preferred_element_type=jnp.float32
    ).astype(jnp.bfloat16)
    key_heads = keyval[:, 0].reshape(block_len, heads_here, HDIM)
    value_heads = keyval[:, 1].reshape(block_len, heads_here, HDIM)
    query_heads = queries.reshape(total_rows, heads_here, HDIM)
    scores = jnp.einsum(
        "rhc,thc->hrt", query_heads, key_heads, preferred_element_type=jnp.float32
    ) * HDIM ** (-0.5)
    local_top = jnp.max(scores, axis=2)
    exponent = jnp.exp(scores - local_top[:, :, None])
    weights = exponent.astype(jnp.bfloat16)
    numerator = jnp.einsum(
        "hrt,thc->rhc", weights, value_heads, preferred_element_type=jnp.float32
    ).reshape(total_rows, head_columns)
    denominator = jnp.sum(exponent, axis=2).T
    packed = jnp.concatenate([numerator, local_top.T, denominator], axis=1)

    def att_combine(a, b):
        na, ma, da = jnp.split(a, [head_columns, head_columns + heads_here], axis=-1)
        nb_, mb, db = jnp.split(b, [head_columns, head_columns + heads_here], axis=-1)
        top = jnp.maximum(ma, mb)
        sa = jnp.exp(ma - top)
        sb = jnp.exp(mb - top)
        lead = na.shape[:-1]
        num = (
            na.reshape(lead + (heads_here, HDIM)) * sa[..., None]
            + nb_.reshape(lead + (heads_here, HDIM)) * sb[..., None]
        ).reshape(lead + (head_columns,))
        return jnp.concatenate([num, top, da * sa + db * sb], axis=-1)

    combined = _reduce_scatter(
        packed.reshape(n_ctx, slot_count, packed.shape[1]), "ctx", n_ctx, att_combine
    )
    num = combined[:, :head_columns].reshape(slot_count, heads_here, HDIM)
    den = combined[:, head_columns + heads_here :]
    attended = (num / den[:, :, None]).reshape(slot_count, head_columns).astype(jnp.bfloat16)
    attended = _all_gather(attended, "ctx", n_ctx).reshape(total_rows, head_columns)
    attended = _all_gather(attended, "head", n_head)
    attended = attended.transpose(1, 0, 2).reshape(total_rows, n_head * head_columns)

    share = total_rows // n_head
    head_idx = lax.axis_index("head")
    my_rows = lax.dynamic_slice_in_dim(attended, head_idx * share, share, 0)
    branch = jnp.dot(my_rows, out_full, preferred_element_type=jnp.float32)
    branch = _all_gather(branch, "ctx", n_ctx).transpose(1, 0, 2).reshape(share, width)
    meansquare = jnp.mean(branch * branch, axis=1, keepdims=True)
    hidden = (branch * lax.rsqrt(meansquare + 1e-06) * norm_gain).astype(jnp.bfloat16)
    hidden = _all_gather(hidden, "head", n_head).reshape(total_rows, width)

    logits = lax.dot_general(
        hidden, vocab_weight, (((1,), (1,)), ((), ())), preferred_element_type=jnp.float32
    )
    vocab_start = lax.axis_index(("ctx", "head")) * vocab_weight.shape[0]
    vocab_ids = vocab_start + jnp.arange(vocab_weight.shape[0], dtype=jnp.int32)
    local_max = jnp.max(logits, axis=1)
    expsum = jnp.sum(jnp.exp(logits - local_max[:, None]), axis=1)
    picked = jnp.sum(jnp.where(vocab_ids[None, :] == wanted[:, None], logits, 0.0), axis=1)
    stats = jnp.stack([local_max, expsum, picked])

    def lse_combine(a, b):
        top = jnp.maximum(a[0], b[0])
        total = a[1] * jnp.exp(a[0] - top) + b[1] * jnp.exp(b[0] - top)
        return jnp.stack([top, total, a[2] + b[2]])

    stats = _all_reduce(stats, "head", n_head, lse_combine)
    stats = _all_reduce(stats, "ctx", n_ctx, lse_combine)
    losses = (stats[0] + jnp.log(stats[1]) - stats[2]).reshape(n_ctx, slot_count)
    block_losses = lax.dynamic_slice_in_dim(losses, lax.axis_index("ctx"), 1, 0)[0]
    active = jnp.arange(slot_count, dtype=jnp.int32) < mask_count[0]
    return jnp.where(active, block_losses, jnp.zeros_like(block_losses))[None, :]


def solution(mesh):
    in_specs = (
        P("ctx", None),
        P("ctx", "head"),
        P("ctx", None, "head"),
        P("head", "ctx"),
        P(),
        P(("ctx", "head"), None),
        P("ctx", None),
        P("ctx"),
        P("ctx", None),
    )
    out_specs = P("ctx", None)
    return jax.shard_map(shards, mesh=mesh, in_specs=in_specs, out_specs=out_specs, check_vma=False)
```

```python
import jax
import jax.numpy as jnp
from jax import lax
from jax.sharding import PartitionSpec as P

HDIM = 128


def _digits(n):
    b = n.bit_length() - 1
    assert 1 << b == n
    out, p = [], 0
    while p < b:
        r = 4 if b - p >= 2 else 2
        out.append((p, r))
        p += r.bit_length() - 1
    return out


def _swap(x, axis, n, k):
    return lax.ppermute(x, axis, [(j, j ^ k) for j in range(n)])


def _exchange(x_for, axis, n, p, r, digit):
    return [None] + [_swap(x_for(s), axis, n, s << p) for s in range(1, r)]


def _all_reduce(x, axis, n, combine):
    idx = lax.axis_index(axis)
    for p, r in _digits(n):
        digit = (idx // (1 << p)) % r
        got = _exchange(lambda s: x, axis, n, p, r, digit)
        got[0] = x
        stacked = jnp.stack(got)
        acc = lax.dynamic_index_in_dim(stacked, digit, 0, keepdims=False)
        for a in range(1, r):
            acc = combine(acc, lax.dynamic_index_in_dim(stacked, a ^ digit, 0, keepdims=False))
        x = acc
    return x


def _reduce_scatter(x, axis, n, combine):
    idx = lax.axis_index(axis)
    rest = x.shape[1:]
    for p, r in _digits(n):
        digit = (idx // (1 << p)) % r
        x = x.reshape((x.shape[0] // r, r) + rest)
        got = _exchange(
            lambda s: lax.dynamic_index_in_dim(x, digit ^ s, 1, keepdims=False),
            axis, n, p, r, digit,
        )
        acc = lax.dynamic_index_in_dim(x, digit, 1, keepdims=False)
        for s in range(1, r):
            acc = combine(acc, got[s])
        x = acc
    return x[0]


def _all_gather(x, axis, n):
    idx = lax.axis_index(axis)
    rest = x.shape
    for k, (p, r) in enumerate(reversed(_digits(n))):
        digit = (idx // (1 << p)) % r
        got = _exchange(lambda s: x, axis, n, p, r, digit)
        got[0] = x
        stacked = jnp.stack(got)
        x = jnp.stack(
            [lax.dynamic_index_in_dim(stacked, a ^ digit, 0, keepdims=False) for a in range(r)],
            axis=k,
        )
    return x.reshape((n,) + rest)


def _add(a, b):
    return a + b


def shards(
    activations,
    query_weight,
    keyval_weight,
    out_weight,
    norm_gain,
    vocab_weight,
    mask_positions,
    mask_count,
    targets,
):
    n_ctx = lax.axis_size("ctx")
    n_head = lax.axis_size("head")
    block_len = activations.shape[0]
    width = activations.shape[1]
    slot_count = mask_positions.shape[1]
    total_rows = n_ctx * slot_count
    head_columns = query_weight.shape[1]
    heads_here = head_columns // HDIM
    in_rows = query_weight.shape[0]
    col_block = out_weight.shape[1]

    k_weight = lax.all_gather(keyval_weight[:, 0], "ctx", axis=0, tiled=True)
    v_weight = _all_gather(keyval_weight[:, 1], "ctx", n_ctx).reshape(width, head_columns)

    rows_here = jnp.take(activations, mask_positions[0], axis=0)
    row_blocks = lax.all_to_all(rows_here, "ctx", 1, 0, tiled=True)
    partial_q = jnp.dot(row_blocks, query_weight, preferred_element_type=jnp.float32)
    own_q = _reduce_scatter(
        partial_q.reshape(n_ctx, slot_count, head_columns), "ctx", n_ctx, _add
    ).astype(jnp.bfloat16)
    queries = _all_gather(own_q, "ctx", n_ctx).reshape(total_rows, head_columns)

    wanted = _all_gather(targets[0], "ctx", n_ctx).reshape(total_rows)
    out_full = _all_gather(out_weight, "head", n_head).reshape(n_head * head_columns, col_block)

    key_heads = (
        jnp.dot(activations, k_weight, preferred_element_type=jnp.float32)
        .astype(jnp.bfloat16)
        .reshape(block_len, heads_here, HDIM)
    )
    value_heads = (
        jnp.dot(activations, v_weight, preferred_element_type=jnp.float32)
        .astype(jnp.bfloat16)
        .reshape(block_len, heads_here, HDIM)
    )
    query_heads = queries.reshape(total_rows, heads_here, HDIM)
    scores = jnp.einsum(
        "rhc,thc->hrt", query_heads, key_heads, preferred_element_type=jnp.float32
    ) * HDIM ** (-0.5)
    local_top = jnp.max(scores, axis=2)
    exponent = jnp.exp(scores - local_top[:, :, None])
    weights = exponent.astype(jnp.bfloat16)
    numerator = jnp.einsum(
        "hrt,thc->rhc", weights, value_heads, preferred_element_type=jnp.float32
    ).reshape(total_rows, head_columns)
    denominator = jnp.sum(exponent, axis=2).T
    packed = jnp.concatenate([numerator, local_top.T, denominator], axis=1)

    def att_combine(a, b):
        na, ma, da = jnp.split(a, [head_columns, head_columns + heads_here], axis=-1)
        nb_, mb, db = jnp.split(b, [head_columns, head_columns + heads_here], axis=-1)
        top = jnp.maximum(ma, mb)
        sa = jnp.exp(ma - top)
        sb = jnp.exp(mb - top)
        lead = na.shape[:-1]
        num = (
            na.reshape(lead + (heads_here, HDIM)) * sa[..., None]
            + nb_.reshape(lead + (heads_here, HDIM)) * sb[..., None]
        ).reshape(lead + (head_columns,))
        return jnp.concatenate([num, top, da * sa + db * sb], axis=-1)

    combined = _reduce_scatter(
        packed.reshape(n_ctx, slot_count, packed.shape[1]), "ctx", n_ctx, att_combine
    )
    num = combined[:, :head_columns].reshape(slot_count, heads_here, HDIM)
    den = combined[:, head_columns + heads_here :]
    attended = (num / den[:, :, None]).reshape(slot_count, head_columns).astype(jnp.bfloat16)
    attended = _all_gather(attended, "ctx", n_ctx).reshape(total_rows, head_columns)
    attended = _all_gather(attended, "head", n_head)
    attended = attended.transpose(1, 0, 2).reshape(total_rows, n_head * head_columns)

    share = total_rows // n_head
    head_idx = lax.axis_index("head")
    my_rows = lax.dynamic_slice_in_dim(attended, head_idx * share, share, 0)
    branch = jnp.dot(my_rows, out_full, preferred_element_type=jnp.float32)
    sumsq = _all_reduce(jnp.sum(branch * branch, axis=1), "ctx", n_ctx, _add)
    gain = lax.dynamic_slice_in_dim(norm_gain, lax.axis_index("ctx") * col_block, col_block, 0)
    hidden = (
        branch * lax.rsqrt(sumsq / width + 1e-06)[:, None] * gain
    ).astype(jnp.bfloat16)
    hidden = _all_gather(hidden, "ctx", n_ctx).transpose(1, 0, 2).reshape(share, width)
    hidden = _all_gather(hidden, "head", n_head).reshape(total_rows, width)

    logits = lax.dot_general(
        hidden, vocab_weight, (((1,), (1,)), ((), ())), preferred_element_type=jnp.float32
    )
    vocab_start = lax.axis_index(("ctx", "head")) * vocab_weight.shape[0]
    vocab_ids = vocab_start + jnp.arange(vocab_weight.shape[0], dtype=jnp.int32)
    local_max = jnp.max(logits, axis=1)
    expsum = jnp.sum(jnp.exp(logits - local_max[:, None]), axis=1)
    picked = jnp.sum(jnp.where(vocab_ids[None, :] == wanted[:, None], logits, 0.0), axis=1)
    stats = jnp.stack([local_max, expsum, picked])

    def lse_combine(a, b):
        top = jnp.maximum(a[0], b[0])
        total = a[1] * jnp.exp(a[0] - top) + b[1] * jnp.exp(b[0] - top)
        return jnp.stack([top, total, a[2] + b[2]])

    stats = _all_reduce(stats, "head", n_head, lse_combine)
    stats = _all_reduce(stats, "ctx", n_ctx, lse_combine)
    losses = (stats[0] + jnp.log(stats[1]) - stats[2]).reshape(n_ctx, slot_count)
    block_losses = lax.dynamic_slice_in_dim(losses, lax.axis_index("ctx"), 1, 0)[0]
    active = jnp.arange(slot_count, dtype=jnp.int32) < mask_count[0]
    return jnp.where(active, block_losses, jnp.zeros_like(block_losses))[None, :]


def solution(mesh):
    in_specs = (
        P("ctx", None),
        P("ctx", "head"),
        P("ctx", None, "head"),
        P("head", "ctx"),
        P(),
        P(("ctx", "head"), None),
        P("ctx", None),
        P("ctx"),
        P("ctx", None),
    )
    out_specs = P("ctx", None)
    return jax.shard_map(shards, mesh=mesh, in_specs=in_specs, out_specs=out_specs, check_vma=False)
```

```python
import jax
import jax.numpy as jnp
from jax import lax
from jax.sharding import PartitionSpec as P

HDIM = 128


def _digits(n):
    b = n.bit_length() - 1
    assert 1 << b == n
    out, p = [], 0
    while p < b:
        r = 4 if b - p >= 2 else 2
        out.append((p, r))
        p += r.bit_length() - 1
    return out


def _swap(x, axis, n, k):
    return lax.ppermute(x, axis, [(j, j ^ k) for j in range(n)])


def _exchange(x_for, axis, n, p, r, digit):
    return [None] + [_swap(x_for(s), axis, n, s << p) for s in range(1, r)]


def _all_reduce(x, axis, n, combine):
    idx = lax.axis_index(axis)
    for p, r in _digits(n):
        digit = (idx // (1 << p)) % r
        got = _exchange(lambda s: x, axis, n, p, r, digit)
        got[0] = x
        stacked = jnp.stack(got)
        acc = lax.dynamic_index_in_dim(stacked, digit, 0, keepdims=False)
        for a in range(1, r):
            acc = combine(acc, lax.dynamic_index_in_dim(stacked, a ^ digit, 0, keepdims=False))
        x = acc
    return x


def _reduce_scatter(x, axis, n, combine):
    idx = lax.axis_index(axis)
    rest = x.shape[1:]
    for p, r in _digits(n):
        digit = (idx // (1 << p)) % r
        x = x.reshape((x.shape[0] // r, r) + rest)
        got = _exchange(
            lambda s: lax.dynamic_index_in_dim(x, digit ^ s, 1, keepdims=False),
            axis, n, p, r, digit,
        )
        acc = lax.dynamic_index_in_dim(x, digit, 1, keepdims=False)
        for s in range(1, r):
            acc = combine(acc, got[s])
        x = acc
    return x[0]


def _all_gather(x, axis, n):
    idx = lax.axis_index(axis)
    rest = x.shape
    for k, (p, r) in enumerate(reversed(_digits(n))):
        digit = (idx // (1 << p)) % r
        got = _exchange(lambda s: x, axis, n, p, r, digit)
        got[0] = x
        stacked = jnp.stack(got)
        x = jnp.stack(
            [lax.dynamic_index_in_dim(stacked, a ^ digit, 0, keepdims=False) for a in range(r)],
            axis=k,
        )
    return x.reshape((n,) + rest)


def _add(a, b):
    return a + b


def shards(
    activations,
    query_weight,
    keyval_weight,
    out_weight,
    norm_gain,
    vocab_weight,
    mask_positions,
    mask_count,
    targets,
):
    n_ctx = lax.axis_size("ctx")
    n_head = lax.axis_size("head")
    block_len = activations.shape[0]
    width = activations.shape[1]
    slot_count = mask_positions.shape[1]
    total_rows = n_ctx * slot_count
    head_columns = query_weight.shape[1]
    heads_here = head_columns // HDIM
    in_rows = query_weight.shape[0]
    col_block = out_weight.shape[1]

    kv_weight = lax.all_gather(keyval_weight, "ctx", axis=0, tiled=True)

    rows_here = jnp.take(activations, mask_positions[0], axis=0)
    row_blocks = lax.all_to_all(rows_here, "ctx", 1, 0, tiled=True)
    partial_q = jnp.dot(row_blocks, query_weight, preferred_element_type=jnp.float32)
    own_q = _reduce_scatter(
        partial_q.reshape(n_ctx, slot_count, head_columns), "ctx", n_ctx, _add
    ).astype(jnp.bfloat16)
    queries = _all_gather(own_q, "ctx", n_ctx).reshape(total_rows, head_columns)

    wanted = _all_gather(targets[0], "ctx", n_ctx).reshape(total_rows)
    other_vocab = _swap(vocab_weight, "head", n_head, 1) if n_head == 2 else None
    out_full = _all_gather(out_weight, "head", n_head).reshape(n_head * head_columns, col_block)

    keyval = jnp.einsum(
        "td,djc->tjc", activations, kv_weight, preferred_element_type=jnp.float32
    ).astype(jnp.bfloat16)
    key_heads = keyval[:, 0].reshape(block_len, heads_here, HDIM)
    value_heads = keyval[:, 1].reshape(block_len, heads_here, HDIM)
    query_heads = queries.reshape(total_rows, heads_here, HDIM)
    scores = jnp.einsum(
        "rhc,thc->hrt", query_heads, key_heads, preferred_element_type=jnp.float32
    ) * HDIM ** (-0.5)
    local_top = jnp.max(scores, axis=2)
    exponent = jnp.exp(scores - local_top[:, :, None])
    weights = exponent.astype(jnp.bfloat16)
    numerator = jnp.einsum(
        "hrt,thc->rhc", weights, value_heads, preferred_element_type=jnp.float32
    ).reshape(total_rows, head_columns)
    denominator = jnp.sum(exponent, axis=2).T
    packed = jnp.concatenate([numerator, local_top.T, denominator], axis=1)

    def att_combine(a, b):
        na, ma, da = jnp.split(a, [head_columns, head_columns + heads_here], axis=-1)
        nb_, mb, db = jnp.split(b, [head_columns, head_columns + heads_here], axis=-1)
        top = jnp.maximum(ma, mb)
        sa = jnp.exp(ma - top)
        sb = jnp.exp(mb - top)
        lead = na.shape[:-1]
        num = (
            na.reshape(lead + (heads_here, HDIM)) * sa[..., None]
            + nb_.reshape(lead + (heads_here, HDIM)) * sb[..., None]
        ).reshape(lead + (head_columns,))
        return jnp.concatenate([num, top, da * sa + db * sb], axis=-1)

    combined = _reduce_scatter(
        packed.reshape(n_ctx, slot_count, packed.shape[1]), "ctx", n_ctx, att_combine
    )
    num = combined[:, :head_columns].reshape(slot_count, heads_here, HDIM)
    den = combined[:, head_columns + heads_here :]
    attended = (num / den[:, :, None]).reshape(slot_count, head_columns).astype(jnp.bfloat16)
    attended = _all_gather(attended, "ctx", n_ctx).reshape(total_rows, head_columns)
    attended = _all_gather(attended, "head", n_head)
    attended = attended.transpose(1, 0, 2).reshape(total_rows, n_head * head_columns)

    share = total_rows // n_head
    head_idx = lax.axis_index("head")
    my_rows = lax.dynamic_slice_in_dim(attended, head_idx * share, share, 0)
    branch = jnp.dot(my_rows, out_full, preferred_element_type=jnp.float32)
    sumsq = _all_reduce(jnp.sum(branch * branch, axis=1), "ctx", n_ctx, _add)
    gain = lax.dynamic_slice_in_dim(norm_gain, lax.axis_index("ctx") * col_block, col_block, 0)
    hidden = (
        branch * lax.rsqrt(sumsq / width + 1e-06)[:, None] * gain
    ).astype(jnp.bfloat16)
    hidden = _all_gather(hidden, "ctx", n_ctx).transpose(1, 0, 2).reshape(share, width)
    def lse_combine(a, b):
        top = jnp.maximum(a[0], b[0])
        total = a[1] * jnp.exp(a[0] - top) + b[1] * jnp.exp(b[0] - top)
        return jnp.stack([top, total, a[2] + b[2]])

    def shard_stats(rows, shard, shard_index, row_targets):
        logits = lax.dot_general(
            rows, shard, (((1,), (1,)), ((), ())), preferred_element_type=jnp.float32
        )
        ids = shard_index * shard.shape[0] + jnp.arange(shard.shape[0], dtype=jnp.int32)
        top = jnp.max(logits, axis=1)
        total = jnp.sum(jnp.exp(logits - top[:, None]), axis=1)
        picked = jnp.sum(jnp.where(ids[None, :] == row_targets[:, None], logits, 0.0), axis=1)
        return jnp.stack([top, total, picked])

    flat_index = lax.axis_index(("ctx", "head"))
    ctx_idx = lax.axis_index("ctx")
    if other_vocab is not None:
        share_targets = lax.dynamic_slice_in_dim(wanted, head_idx * share, share, 0)
        stats = lse_combine(
            shard_stats(hidden, vocab_weight, flat_index, share_targets),
            shard_stats(hidden, other_vocab, flat_index + 1 - 2 * head_idx, share_targets),
        )
        stats = _all_reduce(stats, "ctx", n_ctx, lse_combine)
        share_losses = stats[0] + jnp.log(stats[1]) - stats[2]
        owner = (ctx_idx * slot_count) // share
        mine = lax.dynamic_slice_in_dim(
            share_losses, ctx_idx * slot_count - owner * share, slot_count, 0
        )
        theirs = _swap(mine, "head", n_head, 1)
        block_losses = jnp.where(owner == head_idx, mine, theirs)
    else:
        hidden = _all_gather(hidden, "head", n_head).reshape(total_rows, width)
        stats = shard_stats(hidden, vocab_weight, flat_index, wanted)
        stats = _all_reduce(stats, "head", n_head, lse_combine)
        stats = _all_reduce(stats, "ctx", n_ctx, lse_combine)
        losses = (stats[0] + jnp.log(stats[1]) - stats[2]).reshape(n_ctx, slot_count)
        block_losses = lax.dynamic_slice_in_dim(losses, ctx_idx, 1, 0)[0]
    active = jnp.arange(slot_count, dtype=jnp.int32) < mask_count[0]
    return jnp.where(active, block_losses, jnp.zeros_like(block_losses))[None, :]


def solution(mesh):
    in_specs = (
        P("ctx", None),
        P("ctx", "head"),
        P("ctx", None, "head"),
        P("head", "ctx"),
        P(),
        P(("ctx", "head"), None),
        P("ctx", None),
        P("ctx"),
        P("ctx", None),
    )
    out_specs = P("ctx", None)
    return jax.shard_map(shards, mesh=mesh, in_specs=in_specs, out_specs=out_specs, check_vma=False)
```

```python
import jax
import jax.numpy as jnp
from jax import lax
from jax.sharding import PartitionSpec as P

HDIM = 128


def _digits(n):
    b = n.bit_length() - 1
    assert 1 << b == n
    out, p = [], 0
    while p < b:
        r = 4 if b - p >= 2 else 2
        out.append((p, r))
        p += r.bit_length() - 1
    return out


def _swap(x, axis, n, k):
    return lax.ppermute(x, axis, [(j, j ^ k) for j in range(n)])


def _exchange(x_for, axis, n, p, r, digit):
    return [None] + [_swap(x_for(s), axis, n, s << p) for s in range(1, r)]


def _all_reduce(x, axis, n, combine):
    idx = lax.axis_index(axis)
    for p, r in _digits(n):
        digit = (idx // (1 << p)) % r
        got = _exchange(lambda s: x, axis, n, p, r, digit)
        got[0] = x
        stacked = jnp.stack(got)
        acc = lax.dynamic_index_in_dim(stacked, digit, 0, keepdims=False)
        for a in range(1, r):
            acc = combine(acc, lax.dynamic_index_in_dim(stacked, a ^ digit, 0, keepdims=False))
        x = acc
    return x


def _reduce_scatter(x, axis, n, combine):
    idx = lax.axis_index(axis)
    rest = x.shape[1:]
    for p, r in _digits(n):
        digit = (idx // (1 << p)) % r
        x = x.reshape((x.shape[0] // r, r) + rest)
        got = _exchange(
            lambda s: lax.dynamic_index_in_dim(x, digit ^ s, 1, keepdims=False),
            axis, n, p, r, digit,
        )
        acc = lax.dynamic_index_in_dim(x, digit, 1, keepdims=False)
        for s in range(1, r):
            acc = combine(acc, got[s])
        x = acc
    return x[0]


def _all_gather(x, axis, n):
    idx = lax.axis_index(axis)
    rest = x.shape
    for k, (p, r) in enumerate(reversed(_digits(n))):
        digit = (idx // (1 << p)) % r
        got = _exchange(lambda s: x, axis, n, p, r, digit)
        got[0] = x
        stacked = jnp.stack(got)
        x = jnp.stack(
            [lax.dynamic_index_in_dim(stacked, a ^ digit, 0, keepdims=False) for a in range(r)],
            axis=k,
        )
    return x.reshape((n,) + rest)


def _add(a, b):
    return a + b


def shards(
    activations,
    query_weight,
    keyval_weight,
    out_weight,
    norm_gain,
    vocab_weight,
    mask_positions,
    mask_count,
    targets,
):
    n_ctx = lax.axis_size("ctx")
    n_head = lax.axis_size("head")
    block_len = activations.shape[0]
    width = activations.shape[1]
    slot_count = mask_positions.shape[1]
    total_rows = n_ctx * slot_count
    head_columns = query_weight.shape[1]
    heads_here = head_columns // HDIM
    in_rows = query_weight.shape[0]
    col_block = out_weight.shape[1]

    kv_weight = lax.all_gather(keyval_weight, "ctx", axis=0, tiled=True)

    rows_here = jnp.take(activations, mask_positions[0], axis=0)
    row_blocks = lax.all_to_all(rows_here, "ctx", 1, 0, tiled=True)
    partial_q = jnp.dot(row_blocks, query_weight, preferred_element_type=jnp.float32)
    own_q = _reduce_scatter(
        partial_q.reshape(n_ctx, slot_count, head_columns), "ctx", n_ctx, _add
    ).astype(jnp.bfloat16)
    queries = _all_gather(own_q, "ctx", n_ctx).reshape(total_rows, head_columns)

    wanted = _all_gather(targets[0], "ctx", n_ctx).reshape(total_rows)
    other_vocab = _swap(vocab_weight, "head", n_head, 1) if n_head == 2 else None

    keyval = jnp.einsum(
        "td,djc->tjc", activations, kv_weight, preferred_element_type=jnp.float32
    ).astype(jnp.bfloat16)
    key_heads = keyval[:, 0].reshape(block_len, heads_here, HDIM)
    value_heads = keyval[:, 1].reshape(block_len, heads_here, HDIM)
    query_heads = queries.reshape(total_rows, heads_here, HDIM)
    scores = jnp.einsum(
        "rhc,thc->hrt", query_heads, key_heads, preferred_element_type=jnp.float32
    ) * HDIM ** (-0.5)
    local_top = jnp.max(scores, axis=2)
    exponent = jnp.exp(scores - local_top[:, :, None])
    weights = exponent.astype(jnp.bfloat16)
    numerator = jnp.einsum(
        "hrt,thc->rhc", weights, value_heads, preferred_element_type=jnp.float32
    ).reshape(total_rows, head_columns)
    denominator = jnp.sum(exponent, axis=2).T
    packed = jnp.concatenate([numerator, local_top.T, denominator], axis=1)

    def att_combine(a, b):
        na, ma, da = jnp.split(a, [head_columns, head_columns + heads_here], axis=-1)
        nb_, mb, db = jnp.split(b, [head_columns, head_columns + heads_here], axis=-1)
        top = jnp.maximum(ma, mb)
        sa = jnp.exp(ma - top)
        sb = jnp.exp(mb - top)
        lead = na.shape[:-1]
        num = (
            na.reshape(lead + (heads_here, HDIM)) * sa[..., None]
            + nb_.reshape(lead + (heads_here, HDIM)) * sb[..., None]
        ).reshape(lead + (head_columns,))
        return jnp.concatenate([num, top, da * sa + db * sb], axis=-1)

    combined = _reduce_scatter(
        packed.reshape(n_ctx, slot_count, packed.shape[1]), "ctx", n_ctx, att_combine
    )
    num = combined[:, :head_columns].reshape(slot_count, heads_here, HDIM)
    den = combined[:, head_columns + heads_here :]
    attended = (num / den[:, :, None]).reshape(slot_count, head_columns).astype(jnp.bfloat16)
    attended = _all_gather(attended, "ctx", n_ctx).reshape(total_rows, head_columns)

    share = total_rows // n_head
    head_idx = lax.axis_index("head")
    partial_branch = jnp.dot(attended, out_weight, preferred_element_type=jnp.float32)
    branch = _reduce_scatter(
        partial_branch.reshape(n_head, share, col_block), "head", n_head, _add
    )
    sumsq = _all_reduce(jnp.sum(branch * branch, axis=1), "ctx", n_ctx, _add)
    gain = lax.dynamic_slice_in_dim(norm_gain, lax.axis_index("ctx") * col_block, col_block, 0)
    hidden = (
        branch * lax.rsqrt(sumsq / width + 1e-06)[:, None] * gain
    ).astype(jnp.bfloat16)
    hidden = _all_gather(hidden, "ctx", n_ctx).transpose(1, 0, 2).reshape(share, width)
    def lse_combine(a, b):
        top = jnp.maximum(a[0], b[0])
        total = a[1] * jnp.exp(a[0] - top) + b[1] * jnp.exp(b[0] - top)
        return jnp.stack([top, total, a[2] + b[2]])

    def shard_stats(rows, shard, shard_index, row_targets):
        logits = lax.dot_general(
            rows, shard, (((1,), (1,)), ((), ())), preferred_element_type=jnp.float32
        )
        ids = shard_index * shard.shape[0] + jnp.arange(shard.shape[0], dtype=jnp.int32)
        top = jnp.max(logits, axis=1)
        total = jnp.sum(jnp.exp(logits - top[:, None]), axis=1)
        picked = jnp.sum(jnp.where(ids[None, :] == row_targets[:, None], logits, 0.0), axis=1)
        return jnp.stack([top, total, picked])

    flat_index = lax.axis_index(("ctx", "head"))
    ctx_idx = lax.axis_index("ctx")
    if other_vocab is not None:
        share_targets = lax.dynamic_slice_in_dim(wanted, head_idx * share, share, 0)
        stats = lse_combine(
            shard_stats(hidden, vocab_weight, flat_index, share_targets),
            shard_stats(hidden, other_vocab, flat_index + 1 - 2 * head_idx, share_targets),
        )
        stats = _all_reduce(stats, "ctx", n_ctx, lse_combine)
        share_losses = stats[0] + jnp.log(stats[1]) - stats[2]
        owner = (ctx_idx * slot_count) // share
        mine = lax.dynamic_slice_in_dim(
            share_losses, ctx_idx * slot_count - owner * share, slot_count, 0
        )
        theirs = _swap(mine, "head", n_head, 1)
        block_losses = jnp.where(owner == head_idx, mine, theirs)
    else:
        hidden = _all_gather(hidden, "head", n_head).reshape(total_rows, width)
        stats = shard_stats(hidden, vocab_weight, flat_index, wanted)
        stats = _all_reduce(stats, "head", n_head, lse_combine)
        stats = _all_reduce(stats, "ctx", n_ctx, lse_combine)
        losses = (stats[0] + jnp.log(stats[1]) - stats[2]).reshape(n_ctx, slot_count)
        block_losses = lax.dynamic_slice_in_dim(losses, ctx_idx, 1, 0)[0]
    active = jnp.arange(slot_count, dtype=jnp.int32) < mask_count[0]
    return jnp.where(active, block_losses, jnp.zeros_like(block_losses))[None, :]


def solution(mesh):
    in_specs = (
        P("ctx", None),
        P("ctx", "head"),
        P("ctx", None, "head"),
        P("head", "ctx"),
        P(),
        P(("ctx", "head"), None),
        P("ctx", None),
        P("ctx"),
        P("ctx", None),
    )
    out_specs = P("ctx", None)
    return jax.shard_map(shards, mesh=mesh, in_specs=in_specs, out_specs=out_specs, check_vma=False)
```

```python
import jax
import jax.numpy as jnp
from jax import lax
from jax.experimental import pallas as pl
from jax.experimental.pallas import tpu as pltpu
from jax.sharding import PartitionSpec as P

HDIM = 128


def _digits(n):
    b = n.bit_length() - 1
    assert 1 << b == n
    out, p = [], 0
    while p < b:
        r = 4 if b - p >= 2 else 2
        out.append((p, r))
        p += r.bit_length() - 1
    return out


def _swap(x, axis, n, k):
    return lax.ppermute(x, axis, [(j, j ^ k) for j in range(n)])


def _exchange(x_for, axis, n, p, r, digit):
    return [None] + [_swap(x_for(s), axis, n, s << p) for s in range(1, r)]


def _all_reduce(x, axis, n, combine):
    idx = lax.axis_index(axis)
    for p, r in _digits(n):
        digit = (idx // (1 << p)) % r
        got = _exchange(lambda s: x, axis, n, p, r, digit)
        got[0] = x
        stacked = jnp.stack(got)
        acc = lax.dynamic_index_in_dim(stacked, digit, 0, keepdims=False)
        for a in range(1, r):
            acc = combine(acc, lax.dynamic_index_in_dim(stacked, a ^ digit, 0, keepdims=False))
        x = acc
    return x


def _reduce_scatter(x, axis, n, combine):
    idx = lax.axis_index(axis)
    rest = x.shape[1:]
    for p, r in _digits(n):
        digit = (idx // (1 << p)) % r
        x = x.reshape((x.shape[0] // r, r) + rest)
        got = _exchange(
            lambda s: lax.dynamic_index_in_dim(x, digit ^ s, 1, keepdims=False),
            axis, n, p, r, digit,
        )
        acc = lax.dynamic_index_in_dim(x, digit, 1, keepdims=False)
        for s in range(1, r):
            acc = combine(acc, got[s])
        x = acc
    return x[0]


def _all_gather(x, axis, n):
    idx = lax.axis_index(axis)
    rest = x.shape
    for k, (p, r) in enumerate(reversed(_digits(n))):
        digit = (idx // (1 << p)) % r
        got = _exchange(lambda s: x, axis, n, p, r, digit)
        got[0] = x
        stacked = jnp.stack(got)
        x = jnp.stack(
            [lax.dynamic_index_in_dim(stacked, a ^ digit, 0, keepdims=False) for a in range(r)],
            axis=k,
        )
    return x.reshape((n,) + rest)


def _stats_kernel(h_ref, v_ref, t_ref, m_out, s_out, p_out, m_sc, s_sc, p_sc):
    j = pl.program_id(0)
    tile = v_ref.shape[0]

    @pl.when(j == 0)
    def _():
        m_sc[...] = jnp.full(m_sc.shape, -jnp.inf, jnp.float32)
        s_sc[...] = jnp.zeros(s_sc.shape, jnp.float32)
        p_sc[...] = jnp.zeros(p_sc.shape, jnp.float32)

    lt = lax.dot_general(
        v_ref[...], h_ref[...], (((1,), (1,)), ((), ())), preferred_element_type=jnp.float32
    )
    ids = j * tile + lax.broadcasted_iota(jnp.int32, lt.shape, 0)
    m_old = m_sc[...]
    m_new = jnp.maximum(m_old, jnp.max(lt, axis=0, keepdims=True))
    s_sc[...] = s_sc[...] * jnp.exp(m_old - m_new) + jnp.sum(
        jnp.exp(lt - m_new), axis=0, keepdims=True
    )
    p_sc[...] += jnp.sum(jnp.where(ids == t_ref[...], lt, 0.0), axis=0, keepdims=True)
    m_sc[...] = m_new

    @pl.when(j == pl.num_programs(0) - 1)
    def _():
        m_out[...] = m_sc[...]
        s_out[...] = s_sc[...]
        p_out[...] = p_sc[...]


def _shard_stats_kernel(rows, shard, local_targets):
    n_rows, width = rows.shape
    n_vocab = shard.shape[0]
    tile = n_vocab
    for cand in range(512, 7, -8):
        if n_vocab % cand == 0:
            tile = cand
            break
    row_spec = pl.BlockSpec((1, n_rows), lambda j: (0, 0))
    outs = pl.pallas_call(
        _stats_kernel,
        grid=(n_vocab // tile,),
        in_specs=[
            pl.BlockSpec((n_rows, width), lambda j: (0, 0)),
            pl.BlockSpec((tile, width), lambda j: (j, 0)),
            row_spec,
        ],
        out_specs=[row_spec] * 3,
        out_shape=[jax.ShapeDtypeStruct((1, n_rows), jnp.float32)] * 3,
        scratch_shapes=[pltpu.VMEM((1, n_rows), jnp.float32)] * 3,
        compiler_params=pltpu.CompilerParams(dimension_semantics=("arbitrary",)),
        cost_estimate=pl.CostEstimate(
            flops=2 * n_rows * n_vocab * width,
            transcendentals=n_rows * n_vocab,
            bytes_accessed=2 * (n_vocab + n_rows) * width,
        ),
    )(rows, shard, local_targets[None, :])
    return jnp.concatenate(outs, axis=0)


def _add(a, b):
    return a + b


def shards(
    activations,
    query_weight,
    keyval_weight,
    out_weight,
    norm_gain,
    vocab_weight,
    mask_positions,
    mask_count,
    targets,
):
    n_ctx = lax.axis_size("ctx")
    n_head = lax.axis_size("head")
    block_len = activations.shape[0]
    width = activations.shape[1]
    slot_count = mask_positions.shape[1]
    total_rows = n_ctx * slot_count
    head_columns = query_weight.shape[1]
    heads_here = head_columns // HDIM
    in_rows = query_weight.shape[0]
    col_block = out_weight.shape[1]

    kv_weight = lax.all_gather(keyval_weight, "ctx", axis=0, tiled=True)

    rows_here = jnp.take(activations, mask_positions[0], axis=0)
    row_blocks = lax.all_to_all(rows_here, "ctx", 1, 0, tiled=True)
    partial_q = jnp.dot(row_blocks, query_weight, preferred_element_type=jnp.float32)
    own_q = _reduce_scatter(
        partial_q.reshape(n_ctx, slot_count, head_columns), "ctx", n_ctx, _add
    ).astype(jnp.bfloat16)
    queries = _all_gather(own_q, "ctx", n_ctx).reshape(total_rows, head_columns)

    wanted = _all_gather(targets[0], "ctx", n_ctx).reshape(total_rows)
    other_vocab = _swap(vocab_weight, "head", n_head, 1) if n_head == 2 else None

    keyval = jnp.einsum(
        "td,djc->tjc", activations, kv_weight, preferred_element_type=jnp.float32
    ).astype(jnp.bfloat16)
    key_heads = keyval[:, 0].reshape(block_len, heads_here, HDIM)
    value_heads = keyval[:, 1].reshape(block_len, heads_here, HDIM)
    query_heads = queries.reshape(total_rows, heads_here, HDIM)
    scores = jnp.einsum(
        "rhc,thc->hrt", query_heads, key_heads, preferred_element_type=jnp.float32
    ) * HDIM ** (-0.5)
    local_top = jnp.max(scores, axis=2)
    exponent = jnp.exp(scores - local_top[:, :, None])
    weights = exponent.astype(jnp.bfloat16)
    numerator = jnp.einsum(
        "hrt,thc->rhc", weights, value_heads, preferred_element_type=jnp.float32
    ).reshape(total_rows, head_columns)
    denominator = jnp.sum(exponent, axis=2).T
    packed = jnp.concatenate([numerator, local_top.T, denominator], axis=1)

    def att_combine(a, b):
        na, ma, da = jnp.split(a, [head_columns, head_columns + heads_here], axis=-1)
        nb_, mb, db = jnp.split(b, [head_columns, head_columns + heads_here], axis=-1)
        top = jnp.maximum(ma, mb)
        sa = jnp.exp(ma - top)
        sb = jnp.exp(mb - top)
        lead = na.shape[:-1]
        num = (
            na.reshape(lead + (heads_here, HDIM)) * sa[..., None]
            + nb_.reshape(lead + (heads_here, HDIM)) * sb[..., None]
        ).reshape(lead + (head_columns,))
        return jnp.concatenate([num, top, da * sa + db * sb], axis=-1)

    combined = _reduce_scatter(
        packed.reshape(n_ctx, slot_count, packed.shape[1]), "ctx", n_ctx, att_combine
    )
    num = combined[:, :head_columns].reshape(slot_count, heads_here, HDIM)
    den = combined[:, head_columns + heads_here :]
    attended = (num / den[:, :, None]).reshape(slot_count, head_columns).astype(jnp.bfloat16)
    attended = _all_gather(attended, "ctx", n_ctx).reshape(total_rows, head_columns)

    share = total_rows // n_head
    head_idx = lax.axis_index("head")
    partial_branch = jnp.dot(attended, out_weight, preferred_element_type=jnp.float32)
    branch = _reduce_scatter(
        partial_branch.reshape(n_head, share, col_block), "head", n_head, _add
    )
    sumsq = _all_reduce(jnp.sum(branch * branch, axis=1), "ctx", n_ctx, _add)
    gain = lax.dynamic_slice_in_dim(norm_gain, lax.axis_index("ctx") * col_block, col_block, 0)
    hidden = (
        branch * lax.rsqrt(sumsq / width + 1e-06)[:, None] * gain
    ).astype(jnp.bfloat16)
    hidden = _all_gather(hidden, "ctx", n_ctx).transpose(1, 0, 2).reshape(share, width)
    def lse_combine(a, b):
        top = jnp.maximum(a[0], b[0])
        total = a[1] * jnp.exp(a[0] - top) + b[1] * jnp.exp(b[0] - top)
        return jnp.stack([top, total, a[2] + b[2]])

    def shard_stats(rows, shard, shard_index, row_targets):
        logits = lax.dot_general(
            rows, shard, (((1,), (1,)), ((), ())), preferred_element_type=jnp.float32
        )
        ids = shard_index * shard.shape[0] + jnp.arange(shard.shape[0], dtype=jnp.int32)
        top = jnp.max(logits, axis=1)
        total = jnp.sum(jnp.exp(logits - top[:, None]), axis=1)
        picked = jnp.sum(jnp.where(ids[None, :] == row_targets[:, None], logits, 0.0), axis=1)
        return jnp.stack([top, total, picked])

    flat_index = lax.axis_index(("ctx", "head"))
    ctx_idx = lax.axis_index("ctx")
    if other_vocab is not None:
        share_targets = lax.dynamic_slice_in_dim(wanted, head_idx * share, share, 0)
        n_vocab = vocab_weight.shape[0]
        other_index = flat_index + 1 - 2 * head_idx
        stats = lse_combine(
            _shard_stats_kernel(hidden, vocab_weight, share_targets - flat_index * n_vocab),
            _shard_stats_kernel(hidden, other_vocab, share_targets - other_index * n_vocab),
        )
        stats = _all_reduce(stats, "ctx", n_ctx, lse_combine)
        share_losses = stats[0] + jnp.log(stats[1]) - stats[2]
        owner = (ctx_idx * slot_count) // share
        mine = lax.dynamic_slice_in_dim(
            share_losses, ctx_idx * slot_count - owner * share, slot_count, 0
        )
        theirs = _swap(mine, "head", n_head, 1)
        block_losses = jnp.where(owner == head_idx, mine, theirs)
    else:
        hidden = _all_gather(hidden, "head", n_head).reshape(total_rows, width)
        stats = shard_stats(hidden, vocab_weight, flat_index, wanted)
        stats = _all_reduce(stats, "head", n_head, lse_combine)
        stats = _all_reduce(stats, "ctx", n_ctx, lse_combine)
        losses = (stats[0] + jnp.log(stats[1]) - stats[2]).reshape(n_ctx, slot_count)
        block_losses = lax.dynamic_slice_in_dim(losses, ctx_idx, 1, 0)[0]
    active = jnp.arange(slot_count, dtype=jnp.int32) < mask_count[0]
    return jnp.where(active, block_losses, jnp.zeros_like(block_losses))[None, :]


def solution(mesh):
    in_specs = (
        P("ctx", None),
        P("ctx", "head"),
        P("ctx", None, "head"),
        P("head", "ctx"),
        P(),
        P(("ctx", "head"), None),
        P("ctx", None),
        P("ctx"),
        P("ctx", None),
    )
    out_specs = P("ctx", None)
    return jax.shard_map(shards, mesh=mesh, in_specs=in_specs, out_specs=out_specs, check_vma=False)
```

```python
import jax
import jax.numpy as jnp
from jax import lax
from jax.sharding import PartitionSpec as P

HDIM = 128


def _digits(n):
    b = n.bit_length() - 1
    assert 1 << b == n
    out, p = [], 0
    while p < b:
        r = 4 if b - p >= 2 else 2
        out.append((p, r))
        p += r.bit_length() - 1
    return out


def _swap(x, axis, n, k):
    return lax.ppermute(x, axis, [(j, j ^ k) for j in range(n)])


def _exchange(x_for, axis, n, p, r, digit):
    return [None] + [_swap(x_for(s), axis, n, s << p) for s in range(1, r)]


def _all_reduce(x, axis, n, combine):
    idx = lax.axis_index(axis)
    for p, r in _digits(n):
        digit = (idx // (1 << p)) % r
        got = _exchange(lambda s: x, axis, n, p, r, digit)
        got[0] = x
        stacked = jnp.stack(got)
        acc = lax.dynamic_index_in_dim(stacked, digit, 0, keepdims=False)
        for a in range(1, r):
            acc = combine(acc, lax.dynamic_index_in_dim(stacked, a ^ digit, 0, keepdims=False))
        x = acc
    return x


def _reduce_scatter(x, axis, n, combine):
    idx = lax.axis_index(axis)
    rest = x.shape[1:]
    for p, r in _digits(n):
        digit = (idx // (1 << p)) % r
        x = x.reshape((x.shape[0] // r, r) + rest)
        got = _exchange(
            lambda s: lax.dynamic_index_in_dim(x, digit ^ s, 1, keepdims=False),
            axis, n, p, r, digit,
        )
        acc = lax.dynamic_index_in_dim(x, digit, 1, keepdims=False)
        for s in range(1, r):
            acc = combine(acc, got[s])
        x = acc
    return x[0]


def _all_gather(x, axis, n):
    idx = lax.axis_index(axis)
    rest = x.shape
    for k, (p, r) in enumerate(reversed(_digits(n))):
        digit = (idx // (1 << p)) % r
        got = _exchange(lambda s: x, axis, n, p, r, digit)
        got[0] = x
        stacked = jnp.stack(got)
        x = jnp.stack(
            [lax.dynamic_index_in_dim(stacked, a ^ digit, 0, keepdims=False) for a in range(r)],
            axis=k,
        )
    return x.reshape((n,) + rest)


def _add(a, b):
    return a + b


def shards(
    activations,
    query_weight,
    keyval_weight,
    out_weight,
    norm_gain,
    vocab_weight,
    mask_positions,
    mask_count,
    targets,
):
    n_ctx = lax.axis_size("ctx")
    n_head = lax.axis_size("head")
    block_len = activations.shape[0]
    width = activations.shape[1]
    slot_count = mask_positions.shape[1]
    total_rows = n_ctx * slot_count
    head_columns = query_weight.shape[1]
    heads_here = head_columns // HDIM
    in_rows = query_weight.shape[0]
    col_block = out_weight.shape[1]

    kv_weight = lax.all_gather(keyval_weight, "ctx", axis=0, tiled=True)

    rows_here = jnp.take(activations, mask_positions[0], axis=0)
    row_blocks = lax.all_to_all(rows_here, "ctx", 1, 0, tiled=True)
    partial_q = jnp.dot(row_blocks, query_weight, preferred_element_type=jnp.float32)
    own_q = _reduce_scatter(
        partial_q.reshape(n_ctx, slot_count, head_columns), "ctx", n_ctx, _add
    ).astype(jnp.bfloat16)
    queries = _all_gather(own_q, "ctx", n_ctx).reshape(total_rows, head_columns)

    wanted = _all_gather(targets[0], "ctx", n_ctx).reshape(total_rows)
    other_vocab = _swap(vocab_weight, "head", n_head, 1) if n_head == 2 else None

    keyval = jnp.einsum(
        "td,djc->tjc", activations, kv_weight, preferred_element_type=jnp.float32
    ).astype(jnp.bfloat16)
    key_heads = keyval[:, 0].reshape(block_len, heads_here, HDIM)
    value_heads = keyval[:, 1].reshape(block_len, heads_here, HDIM)
    query_heads = queries.reshape(total_rows, heads_here, HDIM)
    scores = jnp.einsum(
        "rhc,thc->hrt", query_heads, key_heads, preferred_element_type=jnp.float32
    ) * HDIM ** (-0.5)
    local_top = jnp.max(scores, axis=2)
    exponent = jnp.exp(scores - local_top[:, :, None])
    weights = exponent.astype(jnp.bfloat16)
    numerator = jnp.einsum(
        "hrt,thc->rhc", weights, value_heads, preferred_element_type=jnp.float32
    ).reshape(total_rows, head_columns)
    denominator = jnp.sum(exponent, axis=2).T
    packed = jnp.concatenate([numerator, local_top.T, denominator], axis=1)

    def att_combine(a, b):
        na, ma, da = jnp.split(a, [head_columns, head_columns + heads_here], axis=-1)
        nb_, mb, db = jnp.split(b, [head_columns, head_columns + heads_here], axis=-1)
        top = jnp.maximum(ma, mb)
        sa = jnp.exp(ma - top)
        sb = jnp.exp(mb - top)
        lead = na.shape[:-1]
        num = (
            na.reshape(lead + (heads_here, HDIM)) * sa[..., None]
            + nb_.reshape(lead + (heads_here, HDIM)) * sb[..., None]
        ).reshape(lead + (head_columns,))
        return jnp.concatenate([num, top, da * sa + db * sb], axis=-1)

    combined = _reduce_scatter(
        packed.reshape(n_ctx, slot_count, packed.shape[1]), "ctx", n_ctx, att_combine
    )
    num = combined[:, :head_columns].reshape(slot_count, heads_here, HDIM)
    den = combined[:, head_columns + heads_here :]
    attended = (num / den[:, :, None]).reshape(slot_count, head_columns).astype(jnp.bfloat16)
    attended = _all_gather(attended, "ctx", n_ctx).reshape(total_rows, head_columns)

    share = total_rows // n_head
    head_idx = lax.axis_index("head")
    partial_branch = jnp.dot(attended, out_weight, preferred_element_type=jnp.float32)
    branch = _reduce_scatter(
        partial_branch.reshape(n_head, share, col_block), "head", n_head, _add
    )
    sumsq = _all_reduce(jnp.sum(branch * branch, axis=1), "ctx", n_ctx, _add)
    gain = lax.dynamic_slice_in_dim(norm_gain, lax.axis_index("ctx") * col_block, col_block, 0)
    hidden = (
        branch * lax.rsqrt(sumsq / width + 1e-06)[:, None] * gain
    ).astype(jnp.bfloat16)
    def lse_combine(a, b):
        top = jnp.maximum(a[0], b[0])
        total = a[1] * jnp.exp(a[0] - top) + b[1] * jnp.exp(b[0] - top)
        return jnp.stack([top, total, a[2] + b[2]])

    def shard_stats(rows, shard, shard_index, row_targets):
        logits = lax.dot_general(
            rows, shard, (((1,), (1,)), ((), ())), preferred_element_type=jnp.float32
        )
        ids = shard_index * shard.shape[0] + jnp.arange(shard.shape[0], dtype=jnp.int32)
        top = jnp.max(logits, axis=1)
        total = jnp.sum(jnp.exp(logits - top[:, None]), axis=1)
        picked = jnp.sum(jnp.where(ids[None, :] == row_targets[:, None], logits, 0.0), axis=1)
        return jnp.stack([top, total, picked])

    flat_index = lax.axis_index(("ctx", "head"))
    ctx_idx = lax.axis_index("ctx")
    if other_vocab is not None:
        share_targets = lax.dynamic_slice_in_dim(wanted, head_idx * share, share, 0)
        rounds = list(reversed(_digits(n_ctx)))
        p0, r0 = rounds[0]
        low_count = 1 << p0
        low = ctx_idx % low_count
        others = [(low + j) % low_count for j in range(1, low_count)]
        dig0 = (ctx_idx // low_count) % r0
        got = _exchange(lambda s: hidden, "ctx", n_ctx, p0, r0, dig0)
        got[0] = hidden
        stacked = jnp.stack(got)
        first = jnp.stack(
            [lax.dynamic_index_in_dim(stacked, a ^ dig0, 0, keepdims=False) for a in range(r0)]
        )
        x = first
        for k, (p, r) in enumerate(rounds[1:]):
            digit = (ctx_idx // (1 << p)) % r
            got = _exchange(lambda s: x, "ctx", n_ctx, p, r, digit)
            got[0] = x
            stacked = jnp.stack(got)
            x = jnp.stack(
                [lax.dynamic_index_in_dim(stacked, a ^ digit, 0, keepdims=False) for a in range(r)],
                axis=k + 1,
            )
        full = x.reshape((r0, low_count, share, col_block))
        hid_a = first.transpose(1, 0, 2).reshape(share, r0 * col_block)
        hid_b = jnp.stack(
            [lax.dynamic_index_in_dim(full, o, 1, keepdims=False) for o in others], axis=1
        )
        hid_b = hid_b.transpose(2, 0, 1, 3).reshape(share, width - r0 * col_block)

        def split_stats(shard, shard_index):
            n_vocab = shard.shape[0]
            v4 = shard.reshape(n_vocab, r0, low_count, col_block)
            voc_a = lax.dynamic_index_in_dim(v4, low, 2, keepdims=False).reshape(n_vocab, -1)
            voc_b = jnp.stack(
                [lax.dynamic_index_in_dim(v4, o, 2, keepdims=False) for o in others], axis=2
            ).reshape(n_vocab, -1)
            dims = (((1,), (1,)), ((), ()))
            logits = lax.dot_general(
                hid_a, voc_a, dims, preferred_element_type=jnp.float32
            ) + lax.dot_general(hid_b, voc_b, dims, preferred_element_type=jnp.float32)
            ids = shard_index * n_vocab + jnp.arange(n_vocab, dtype=jnp.int32)
            top = jnp.max(logits, axis=1)
            total = jnp.sum(jnp.exp(logits - top[:, None]), axis=1)
            picked = jnp.sum(
                jnp.where(ids[None, :] == share_targets[:, None], logits, 0.0), axis=1
            )
            return jnp.stack([top, total, picked])

        stats = lse_combine(
            split_stats(vocab_weight, flat_index),
            split_stats(other_vocab, flat_index + 1 - 2 * head_idx),
        )
        stats = _all_reduce(stats, "ctx", n_ctx, lse_combine)
        share_losses = stats[0] + jnp.log(stats[1]) - stats[2]
        owner = (ctx_idx * slot_count) // share
        mine = lax.dynamic_slice_in_dim(
            share_losses, ctx_idx * slot_count - owner * share, slot_count, 0
        )
        theirs = _swap(mine, "head", n_head, 1)
        block_losses = jnp.where(owner == head_idx, mine, theirs)
    else:
        hidden = _all_gather(hidden, "ctx", n_ctx).transpose(1, 0, 2).reshape(share, width)
        hidden = _all_gather(hidden, "head", n_head).reshape(total_rows, width)
        stats = shard_stats(hidden, vocab_weight, flat_index, wanted)
        stats = _all_reduce(stats, "head", n_head, lse_combine)
        stats = _all_reduce(stats, "ctx", n_ctx, lse_combine)
        losses = (stats[0] + jnp.log(stats[1]) - stats[2]).reshape(n_ctx, slot_count)
        block_losses = lax.dynamic_slice_in_dim(losses, ctx_idx, 1, 0)[0]
    active = jnp.arange(slot_count, dtype=jnp.int32) < mask_count[0]
    return jnp.where(active, block_losses, jnp.zeros_like(block_losses))[None, :]


def solution(mesh):
    in_specs = (
        P("ctx", None),
        P("ctx", "head"),
        P("ctx", None, "head"),
        P("head", "ctx"),
        P(),
        P(("ctx", "head"), None),
        P("ctx", None),
        P("ctx"),
        P("ctx", None),
    )
    out_specs = P("ctx", None)
    return jax.shard_map(shards, mesh=mesh, in_specs=in_specs, out_specs=out_specs, check_vma=False)
```
